512 devices in a mesh: seq: 32 (over y_hi, z, core), chan: 16 (over x, y_lo).
Axes of the slice: x: 4, y: 8 (y_hi: 2, y_lo: 4; y = y_hi * 4 + y_lo), z: 8, core: 2. Of those that a mesh axis runs over, the one named last changes fastest.
Arguments:
- signal: bfloat16 [2048, 32768], P('chan', 'seq'), may hold values from -6 to 6
- spectrum: bfloat16 [2, 2048, 64, 1024], P(None, 'chan', 'seq'), may hold values from -5 to 5
- skip_gain: float32 [2048], P('chan'), may hold values from -4 to 4
Outputs:
- filtered: bfloat16 [2048, 32768], P('chan', 'seq')
The draws below stay inside these ranges and needn't reach their ends.
All inputs are finite; a program needn't handle non-finite values.
Results may differ from the reference program's by a relative error of at most 0.001.
Values may be sent and summed in bfloat16 or wider, within the bound.
No kernel may reach another device: no remote copies, remote signals or barrier semaphores. Data moves between devices by JAX's collectives and lax.ppermute only.
A program may use at most 64 MiB of HBM per device.

```python
import math
import jax
import jax.numpy as jnp
from jax import lax

CH = 2048
TOK_DEV = 1024
L = 32768
KM = 64
N_SEQ = 32


def shard_levels(rng, dims, split, smallest, largest):
    def one(dim, shards_of):
        steps = jax.random.uniform(jax.random.fold_in(jax.random.fold_in(rng, 6), dim), (shards_of,), jnp.float32, smallest / len(split), largest / len(split))
        return jnp.repeat(jnp.exp(steps), dims[dim] // shards_of).reshape((-1,) + (1,) * (len(dims) - dim - 1))

    gain = one(*split[0])
    for cut in split[1:]:
        gain = gain * one(*cut)
    return gain


def gaussian(rng, dims, spread, reach, cuts=(), kind=jnp.bfloat16):
    values = spread * jax.random.normal(rng, dims, jnp.float32)
    if cuts:
        values = values * shard_levels(rng, dims, cuts, -0.22, 0.18)
    return jnp.clip(values, -reach, reach).astype(kind)


def setup_inputs(seed: int = 0) -> dict:
    key_of = jax.random.split(jax.random.key(seed), 4)
    return {
        "signal": gaussian(key_of[0], (CH, L), 1.0, 6.0, ((0, 16), (1, 32))),
        "spectrum": gaussian(key_of[1], (2, CH, KM, TOK_DEV), 1.0, 5.0, ((1, 16), (2, 32))),
        "skip_gain": gaussian(key_of[2], (CH,), 1.0, 4.0, ((0, 16),), jnp.float32),
    }


def reference(signal, spectrum, skip_gain):
    length = TOK_DEV * N_SEQ
    full_len = 2 * length
    block_rows = math.gcd(CH, 64)
    block_count = CH // block_rows

    def one_block(block_index):
        start = (block_index * block_rows).astype(jnp.int32)
        values = lax.dynamic_slice_in_dim(signal, start, block_rows, 0).astype(jnp.float32)
        stored = lax.dynamic_slice_in_dim(spectrum, start, block_rows, 1).astype(jnp.float32)
        stored = jnp.transpose(stored, (0, 1, 3, 2)).reshape(2, block_rows, full_len)
        gains = lax.dynamic_slice_in_dim(skip_gain, start, block_rows, 0)
        forward = jnp.fft.fft(values, n=full_len, axis=1)
        product = forward * (stored[0] + 1j * stored[1])
        convolved = jnp.real(jnp.fft.ifft(product, axis=1))[:, :length]
        return (convolved + gains[:, None] * values).astype(jnp.bfloat16)

    outputs = lax.map(one_block, jnp.arange(block_count, dtype=jnp.int32))
    return outputs.reshape(CH, length)
```

```python
import math

import jax
import jax.numpy as jnp
from jax import lax
from jax.sharding import PartitionSpec as P


def product_hi(form, left, right):
    return jnp.einsum(form, left, right, precision=lax.Precision.HIGHEST)


def phase_of(numer, denom):
    angle = 2.0 * math.pi / denom * (numer % denom).astype(jnp.float32)
    return (jnp.cos(angle), jnp.sin(angle))


def local_conv(x, s, gain):
    count, length = x.shape
    full_len = 2 * length
    n1_len, n2_len = s.shape[2], s.shape[3]
    half1 = length // n2_len
    ids1 = jnp.arange(n1_len, dtype=jnp.int32)
    ids2 = jnp.arange(n2_len, dtype=jnp.int32)
    c1, s1 = phase_of(ids1[:, None] * ids1[None, :], n1_len)
    c2, s2 = phase_of(ids2[:, None] * ids2[None, :], n2_len)
    tc, ts = phase_of(ids1[:, None] * ids2[None, :], full_len)
    xr = x.reshape(count, half1, n2_len)
    ar = product_hi("kn,cnm->ckm", c1[:, :half1], xr)
    ai = -product_hi("kn,cnm->ckm", s1[:, :half1], xr)
    br = ar * tc + ai * ts
    bi = ai * tc - ar * ts
    xfr = product_hi("ckn,nj->ckj", br, c2) + product_hi("ckn,nj->ckj", bi, s2)
    xfi = product_hi("ckn,nj->ckj", bi, c2) - product_hi("ckn,nj->ckj", br, s2)
    pr = xfr * s[0] - xfi * s[1]
    pi = xfr * s[1] + xfi * s[0]
    qr = product_hi("ckj,jn->ckn", pr, c2) - product_hi("ckj,jn->ckn", pi, s2)
    qi = product_hi("ckj,jn->ckn", pi, c2) + product_hi("ckj,jn->ckn", pr, s2)
    rr = qr * tc - qi * ts
    ri = qi * tc + qr * ts
    y = product_hi("nk,ckm->cnm", c1[:half1], rr) - product_hi("nk,ckm->cnm", s1[:half1], ri)
    y = y.reshape(count, length) * (1.0 / full_len)
    return (y + gain[:, None] * x).astype(jnp.bfloat16)


def per_device(signal, spectrum, skip_gain):
    ch_blk, slab = signal.shape
    parts = lax.axis_size("seq")
    cpd = ch_blk // parts
    a_loc, nb = spectrum.shape[2], spectrum.shape[3]
    seq_rank = lax.axis_index("seq")
    sig = signal.reshape(parts, cpd, slab)
    spc = spectrum.reshape(2, parts, cpd, a_loc, nb).transpose(1, 2, 0, 3, 4)
    spc = spc.reshape(parts, cpd, 2 * a_loc * nb)
    buf = jnp.concatenate([sig, spc], axis=2)
    got = lax.all_to_all(buf, "seq", 0, 0, tiled=True)
    x = got[:, :, :slab].transpose(1, 0, 2).reshape(cpd, parts * slab).astype(jnp.float32)
    full_len = 2 * parts * slab
    n1_len = 1 << (int(math.log2(full_len)) // 2)
    n2_len = full_len // n1_len
    rep = n1_len // (parts * a_loc)
    cols = jnp.arange(nb, dtype=jnp.int32)
    perm = (cols[:, None] == (cols[None, :] % n2_len) * rep + cols[None, :] // n2_len)
    s = got[:, :, slab:].reshape(parts, cpd, 2, a_loc, nb)
    s = jnp.einsum("pcrab,bq->pcraq", s, perm.astype(jnp.bfloat16),
                   preferred_element_type=jnp.float32)
    s = s.reshape(parts, cpd, 2, a_loc, rep, n2_len).transpose(2, 1, 4, 0, 3, 5)
    s = s.reshape(2, cpd, n1_len, n2_len)
    gain = lax.dynamic_slice_in_dim(skip_gain, seq_rank * cpd, cpd)
    out = local_conv(x, s, gain)
    back = out.reshape(cpd, parts, slab).transpose(1, 0, 2)
    back = lax.all_to_all(back, "seq", 0, 0, tiled=True)
    return back.reshape(ch_blk, slab)


def solution(mesh):
    return jax.shard_map(
        per_device,
        mesh=mesh,
        in_specs=(P("chan", "seq"), P(None, "chan", "seq", None), P("chan")),
        out_specs=P("chan", "seq"),
        check_vma=False,
    )
```

```python
import math

import jax
import jax.numpy as jnp
from jax import lax
from jax.sharding import PartitionSpec as P


def dot_hi(form, left, right):
    return jnp.einsum(form, left, right, precision=lax.Precision.HIGH,
                      preferred_element_type=jnp.float32)


def angle_of(numer, denom):
    return 2.0 * math.pi / denom * (numer % denom).astype(jnp.float32)


def local_conv(x, s, gain, n1_len, km):
    count, length = x.shape
    full_len = 2 * length
    n2_len = full_len // n1_len
    half1 = length // n2_len
    rep = n1_len // km
    rows = jnp.arange(n1_len, dtype=jnp.int32)
    k1 = rows // rep + km * (rows % rep)
    ids2 = jnp.arange(n2_len, dtype=jnp.int32)
    n1 = jnp.arange(half1, dtype=jnp.int32)
    angles = jnp.concatenate([
        angle_of(k1[:, None] * jnp.pad(n1, (0, n2_len - half1))[None, :], n1_len),
        angle_of(ids2[:, None] * ids2[None, :], n2_len),
        angle_of(k1[:, None] * ids2[None, :], full_len),
    ], axis=0)
    tab_c, tab_s = lax.optimization_barrier((jnp.cos(angles), jnp.sin(angles)))
    f1c, f1s = tab_c[:n1_len, :half1], tab_s[:n1_len, :half1]
    wc, ws = tab_c[n1_len:n1_len + n2_len], tab_s[n1_len:n1_len + n2_len]
    tc, ts = tab_c[n1_len + n2_len:], tab_s[n1_len + n2_len:]
    xr = x.reshape(count, half1, n2_len)
    f1 = jnp.stack([f1c, -f1s])
    a = dot_hi("zkn,cnm->zckm", f1, xr)
    ar, ai = a[0], a[1]
    br = ar * tc + ai * ts
    bi = ai * tc - ar * ts
    w = jnp.stack([wc, ws])
    xf = dot_hi("zckn,wnj->zwckj", jnp.stack([br, bi]), w)
    xfr = xf[0, 0] + xf[1, 1]
    xfi = xf[1, 0] - xf[0, 1]
    pr = xfr * s[0] - xfi * s[1]
    pi = xfr * s[1] + xfi * s[0]
    q = dot_hi("zckj,wjn->zwckn", jnp.stack([pr, pi]), w)
    qr = q[0, 0] - q[1, 1]
    qi = q[1, 0] + q[0, 1]
    rr = qr * tc - qi * ts
    ri = qi * tc + qr * ts
    y = dot_hi("zkn,zckm->cnm", jnp.stack([f1c, -f1s]), jnp.stack([rr, ri]))
    y = y.reshape(count, length) * (1.0 / full_len)
    return (y + gain[:, None] * x).astype(jnp.bfloat16)


def per_device(signal, spectrum, skip_gain):
    ch_blk, slab = signal.shape
    parts = lax.axis_size("seq")
    cpd = ch_blk // parts
    a_loc, nb = spectrum.shape[2], spectrum.shape[3]
    km = parts * a_loc
    full_len = 2 * parts * slab
    n1_len = 1 << (int(math.log2(full_len)) // 2)
    n2_len = full_len // n1_len
    rep = n1_len // km
    seq_rank = lax.axis_index("seq")
    sig = signal.reshape(parts, cpd, 1, slab)
    spc = spectrum.reshape(2, parts, cpd, a_loc, nb).transpose(1, 2, 0, 3, 4)
    spc = spc.reshape(parts, cpd, 2 * a_loc, nb)
    buf = jnp.concatenate([sig, spc], axis=2)
    got = lax.all_to_all(buf, "seq", 0, 0, tiled=True)
    x = got[:, :, 0].transpose(1, 0, 2).reshape(cpd, parts * slab).astype(jnp.float32)
    cols = jnp.arange(nb, dtype=jnp.int32)
    perm = cols[:, None] == (cols[None, :] % n2_len) * rep + cols[None, :] // n2_len
    s = jnp.einsum("pcrb,bq->pcrq", got[:, :, 1:], perm.astype(jnp.bfloat16),
                   preferred_element_type=jnp.float32)
    s = s.reshape(parts, cpd, 2, a_loc, nb).transpose(2, 1, 0, 3, 4)
    s = s.reshape(2, cpd, n1_len, n2_len)
    gain = lax.dynamic_slice_in_dim(skip_gain, seq_rank * cpd, cpd)
    out = local_conv(x, s, gain, n1_len, km)
    back = out.reshape(cpd, parts, slab).transpose(1, 0, 2)
    back = lax.all_to_all(back, "seq", 0, 0, tiled=True)
    return back.reshape(ch_blk, slab)


def solution(mesh):
    return jax.shard_map(
        per_device,
        mesh=mesh,
        in_specs=(P("chan", "seq"), P(None, "chan", "seq", None), P("chan")),
        out_specs=P("chan", "seq"),
        check_vma=False,
    )
```

```python
import math

import jax
import jax.numpy as jnp
from jax import lax
from jax.sharding import PartitionSpec as P


def dot_hi(form, left, right):
    return jnp.einsum(form, left, right, precision=lax.Precision.HIGH,
                      preferred_element_type=jnp.float32)


def angle_of(numer, denom):
    return 2.0 * math.pi / denom * (numer % denom).astype(jnp.float32)


def local_conv(x, s, gain, n1_len, km):
    count, length = x.shape
    full_len = 2 * length
    n2_len = full_len // n1_len
    half1 = length // n2_len
    rep = n1_len // km
    rows = jnp.arange(n1_len, dtype=jnp.int32)
    k1 = rows // rep + km * (rows % rep)
    ids2 = jnp.arange(n2_len, dtype=jnp.int32)
    n1 = jnp.arange(half1, dtype=jnp.int32)
    angles = jnp.concatenate([
        angle_of(k1[:, None] * jnp.pad(n1, (0, n2_len - half1))[None, :], n1_len),
        angle_of(ids2[:, None] * ids2[None, :], n2_len),
        angle_of(k1[:, None] * ids2[None, :], full_len),
    ], axis=0)
    tab_c, tab_s = lax.optimization_barrier((jnp.cos(angles), jnp.sin(angles)))
    f1c, f1s = tab_c[:n1_len, :half1], tab_s[:n1_len, :half1]
    wc, ws = tab_c[n1_len:n1_len + n2_len], tab_s[n1_len:n1_len + n2_len]
    tc, ts = tab_c[n1_len + n2_len:], tab_s[n1_len + n2_len:]
    xr = x.reshape(count, half1, n2_len)
    f1 = jnp.stack([f1c, -f1s])
    f1_top = lax.reduce_precision(f1, exponent_bits=8, mantissa_bits=7)
    f1_hi = f1_top.astype(jnp.bfloat16)
    f1_lo = (f1 - f1_top).astype(jnp.bfloat16)
    a = jnp.einsum("hzkn,cnm->hzckm", jnp.stack([f1_hi, f1_lo]), xr,
                   preferred_element_type=jnp.float32)
    ar, ai = a[0, 0] + a[1, 0], a[0, 1] + a[1, 1]
    br = ar * tc + ai * ts
    bi = ai * tc - ar * ts
    w = jnp.stack([wc, ws])
    xf = dot_hi("zckn,wnj->zwckj", jnp.stack([br, bi]), w)
    xfr = xf[0, 0] + xf[1, 1]
    xfi = xf[1, 0] - xf[0, 1]
    pr = xfr * s[0] - xfi * s[1]
    pi = xfr * s[1] + xfi * s[0]
    q = dot_hi("zckj,wjn->zwckn", jnp.stack([pr, pi]), w)
    qr = q[0, 0] - q[1, 1]
    qi = q[1, 0] + q[0, 1]
    rr = qr * tc - qi * ts
    ri = qi * tc + qr * ts
    y = dot_hi("zkn,zckm->cnm", jnp.stack([f1c, -f1s]), jnp.stack([rr, ri]))
    y = y.reshape(count, length) * (1.0 / full_len)
    return (y + gain[:, None] * x.astype(jnp.float32)).astype(jnp.bfloat16)


def per_device(signal, spectrum, skip_gain):
    ch_blk, slab = signal.shape
    parts = lax.axis_size("seq")
    cpd = ch_blk // parts
    a_loc, nb = spectrum.shape[2], spectrum.shape[3]
    km = parts * a_loc
    full_len = 2 * parts * slab
    n1_len = 1 << (int(math.log2(full_len)) // 2)
    n2_len = full_len // n1_len
    rep = n1_len // km
    seq_rank = lax.axis_index("seq")
    cols = jnp.arange(nb, dtype=jnp.int32)
    perm = cols[:, None] == (cols[None, :] % n2_len) * rep + cols[None, :] // n2_len
    spc = jnp.einsum("rcab,bq->rcaq", spectrum, perm.astype(jnp.bfloat16),
                     preferred_element_type=jnp.float32).astype(jnp.bfloat16)
    spc = spc.reshape(2, parts, cpd, a_loc, nb).transpose(1, 2, 0, 3, 4)
    spc = spc.reshape(parts, cpd, 2 * a_loc, nb)
    sig = signal.reshape(parts, cpd, 1, slab)
    buf = jnp.concatenate([sig, spc], axis=2)
    got = lax.all_to_all(buf, "seq", 0, 0, tiled=True)
    x = got[:, :, 0].transpose(1, 0, 2).reshape(cpd, parts * slab)
    s = got[:, :, 1:].reshape(parts, cpd, 2, a_loc, rep, n2_len).astype(jnp.float32)
    s = s.transpose(2, 1, 0, 3, 4, 5).reshape(2, cpd, n1_len, n2_len)
    gain = lax.dynamic_slice_in_dim(skip_gain, seq_rank * cpd, cpd)
    out = local_conv(x, s, gain, n1_len, km)
    back = out.reshape(cpd, parts, slab).transpose(1, 0, 2)
    back = lax.all_to_all(back, "seq", 0, 0, tiled=True)
    return back.reshape(ch_blk, slab)


def solution(mesh):
    return jax.shard_map(
        per_device,
        mesh=mesh,
        in_specs=(P("chan", "seq"), P(None, "chan", "seq", None), P("chan")),
        out_specs=P("chan", "seq"),
        check_vma=False,
    )
```

```python
import math

import jax
import jax.numpy as jnp
from jax import lax
from jax.sharding import PartitionSpec as P


def dot_hi(form, left, right):
    return jnp.einsum(form, left, right, precision=lax.Precision.HIGH,
                      preferred_element_type=jnp.float32)


def angle_of(numer, denom):
    return 2.0 * math.pi / denom * (numer % denom).astype(jnp.float32)


def local_conv(x, s, gain, n1_len, km):
    count, length = x.shape
    full_len = 2 * length
    n2_len = full_len // n1_len
    half1 = length // n2_len
    rep = n1_len // km
    rows = jnp.arange(n1_len, dtype=jnp.int32)
    k1 = rows // rep + km * (rows % rep)
    ids2 = jnp.arange(n2_len, dtype=jnp.int32)
    n1 = jnp.arange(half1, dtype=jnp.int32)
    angles = jnp.concatenate([
        angle_of(k1[:, None] * jnp.pad(n1, (0, n2_len - half1))[None, :], n1_len),
        angle_of(ids2[:, None] * ids2[None, :], n2_len),
        angle_of(k1[:, None] * ids2[None, :], full_len),
    ], axis=0)
    tab_c, tab_s = lax.optimization_barrier((jnp.cos(angles), jnp.sin(angles)))
    f1c, f1s = tab_c[:n1_len, :half1], tab_s[:n1_len, :half1]
    wc, ws = tab_c[n1_len:n1_len + n2_len], tab_s[n1_len:n1_len + n2_len]
    tc, ts = tab_c[n1_len + n2_len:], tab_s[n1_len + n2_len:]
    xr = x.reshape(count, half1, n2_len)
    f1 = jnp.stack([f1c, -f1s])
    f1_top = lax.reduce_precision(f1, exponent_bits=8, mantissa_bits=7)
    f1_hi = f1_top.astype(jnp.bfloat16)
    f1_lo = (f1 - f1_top).astype(jnp.bfloat16)
    a = jnp.einsum("hzkn,cnm->hzckm", jnp.stack([f1_hi, f1_lo]), xr,
                   preferred_element_type=jnp.float32)
    ar, ai = a[0, 0] + a[1, 0], a[0, 1] + a[1, 1]
    br = ar * tc + ai * ts
    bi = ai * tc - ar * ts
    w = jnp.stack([wc, ws])
    xf = dot_hi("zckn,wnj->zwckj", jnp.stack([br, bi]), w)
    xfr = xf[0, 0] + xf[1, 1]
    xfi = xf[1, 0] - xf[0, 1]
    pr = xfr * s[0] - xfi * s[1]
    pi = xfr * s[1] + xfi * s[0]
    q = dot_hi("zckj,wjn->zwckn", jnp.stack([pr, pi]), w)
    qr = q[0, 0] - q[1, 1]
    qi = q[1, 0] + q[0, 1]
    rr = qr * tc - qi * ts
    ri = qi * tc + qr * ts
    y = dot_hi("zkn,zckm->cnm", jnp.stack([f1c, -f1s]), jnp.stack([rr, ri]))
    y = y.reshape(count, length) * (1.0 / full_len)
    return (y + gain[:, None] * x.astype(jnp.float32)).astype(jnp.bfloat16)


def per_device(signal, spectrum, skip_gain):
    ch_blk, slab = signal.shape
    parts = lax.axis_size("seq")
    cpd = ch_blk // parts
    a_loc, nb = spectrum.shape[2], spectrum.shape[3]
    km = parts * a_loc
    full_len = 2 * parts * slab
    n1_len = 1 << (int(math.log2(full_len)) // 2)
    n2_len = full_len // n1_len
    rep = n1_len // km
    seq_rank = lax.axis_index("seq")
    cols = jnp.arange(nb, dtype=jnp.int32)
    perm = cols[:, None] == (cols[None, :] % n2_len) * rep + cols[None, :] // n2_len
    spc = jnp.einsum("rcab,bq->rcaq", spectrum, perm.astype(jnp.bfloat16),
                     preferred_element_type=jnp.float32).astype(jnp.bfloat16)
    spc = spc.reshape(2, parts, cpd, a_loc * rep, n2_len).transpose(1, 2, 0, 3, 4)
    spc = spc.reshape(parts, cpd, 2 * a_loc * rep, n2_len)
    sig = signal.reshape(parts, cpd, slab // n2_len, n2_len)
    buf = jnp.concatenate([spc, sig], axis=2)
    got = lax.all_to_all(buf, "seq", 0, 0, tiled=True)
    spec_rows = 2 * a_loc * rep
    x = got[:, :, spec_rows:].transpose(1, 0, 2, 3).reshape(cpd, parts * slab)
    s = got[:, :, :spec_rows].reshape(parts, cpd, 2, a_loc * rep, n2_len).astype(jnp.float32)
    s = s.transpose(2, 1, 0, 3, 4).reshape(2, cpd, n1_len, n2_len)
    gain = lax.dynamic_slice_in_dim(skip_gain, seq_rank * cpd, cpd)
    out = local_conv(x, s, gain, n1_len, km)
    back = out.reshape(cpd, parts, slab).transpose(1, 0, 2)
    back = lax.all_to_all(back, "seq", 0, 0, tiled=True)
    return back.reshape(ch_blk, slab)


def solution(mesh):
    return jax.shard_map(
        per_device,
        mesh=mesh,
        in_specs=(P("chan", "seq"), P(None, "chan", "seq", None), P("chan")),
        out_specs=P("chan", "seq"),
        check_vma=False,
    )
```

```python
import math

import jax
import jax.numpy as jnp
from jax import lax
from jax.sharding import PartitionSpec as P


def dot_hi(form, left, right):
    return jnp.einsum(form, left, right, precision=lax.Precision.HIGH,
                      preferred_element_type=jnp.float32)


def angle_of(numer, denom):
    return 2.0 * math.pi / denom * (numer % denom).astype(jnp.float32)


def local_conv(x, s, gain, n1_len, km):
    n2_len = s.shape[3]
    parts, count = x.shape[0], x.shape[1]
    length = parts * x.shape[2] * x.shape[3]
    full_len = 2 * length
    half1 = length // n2_len
    rep = n1_len // km
    rows = jnp.arange(n1_len, dtype=jnp.int32)
    k1 = rows // rep + km * (rows % rep)
    ids2 = jnp.arange(n2_len, dtype=jnp.int32)
    n1 = jnp.arange(half1, dtype=jnp.int32)
    angles = jnp.concatenate([
        angle_of(k1[:, None] * jnp.pad(n1, (0, n2_len - half1))[None, :], n1_len),
        angle_of(ids2[:, None] * ids2[None, :], n2_len),
        angle_of(k1[:, None] * ids2[None, :], full_len),
    ], axis=0)
    tab_c, tab_s = lax.optimization_barrier((jnp.cos(angles), jnp.sin(angles)))
    f1c, f1s = tab_c[:n1_len, :half1], tab_s[:n1_len, :half1]
    wc, ws = tab_c[n1_len:n1_len + n2_len], tab_s[n1_len:n1_len + n2_len]
    tc, ts = tab_c[n1_len + n2_len:], tab_s[n1_len + n2_len:]
    xr = x
    f1 = jnp.stack([f1c, -f1s])
    f1_top = lax.reduce_precision(f1, exponent_bits=8, mantissa_bits=7)
    f1_hi = f1_top.astype(jnp.bfloat16)
    f1_lo = (f1 - f1_top).astype(jnp.bfloat16)
    f1_hl = jnp.stack([f1_hi, f1_lo]).reshape(2, 2, n1_len, parts, half1 // parts)
    a = jnp.einsum("hzkpi,pcim->hzckm", f1_hl, xr, preferred_element_type=jnp.float32)
    ar, ai = a[0, 0] + a[1, 0], a[0, 1] + a[1, 1]
    br = ar * tc + ai * ts
    bi = ai * tc - ar * ts
    w = jnp.stack([wc, ws])
    xf = dot_hi("zckn,wnj->zwckj", jnp.stack([br, bi]), w)
    xfr = xf[0, 0] + xf[1, 1]
    xfi = xf[1, 0] - xf[0, 1]
    pr = xfr * s[0] - xfi * s[1]
    pi = xfr * s[1] + xfi * s[0]
    q = dot_hi("zckj,wjn->zwckn", jnp.stack([pr, pi]), w)
    qr = q[0, 0] - q[1, 1]
    qi = q[1, 0] + q[0, 1]
    rr = qr * tc - qi * ts
    ri = qi * tc + qr * ts
    y = dot_hi("zkn,zckm->cnm", jnp.stack([f1c, -f1s]), jnp.stack([rr, ri]))
    y = y.reshape(count, length) * (1.0 / full_len)
    xs = x.transpose(1, 0, 2, 3).reshape(count, length).astype(jnp.float32)
    return (y + gain[:, None] * xs).astype(jnp.bfloat16)


def per_device(signal, spectrum, skip_gain):
    ch_blk, slab = signal.shape
    parts = lax.axis_size("seq")
    cpd = ch_blk // parts
    a_loc, nb = spectrum.shape[2], spectrum.shape[3]
    km = parts * a_loc
    full_len = 2 * parts * slab
    n1_len = 1 << (int(math.log2(full_len)) // 2)
    n2_len = full_len // n1_len
    rep = n1_len // km
    seq_rank = lax.axis_index("seq")
    cols = jnp.arange(nb, dtype=jnp.int32)
    perm = cols[:, None] == (cols[None, :] % n2_len) * rep + cols[None, :] // n2_len
    spc = jnp.einsum("rcab,bq->rcaq", spectrum, perm.astype(jnp.bfloat16),
                     preferred_element_type=jnp.float32).astype(jnp.bfloat16)
    spc = spc.reshape(2, parts, cpd, a_loc * rep, n2_len).transpose(1, 2, 0, 3, 4)
    spc = spc.reshape(parts, cpd, 2 * a_loc * rep, n2_len)
    sig = signal.reshape(parts, cpd, slab // n2_len, n2_len)
    buf = jnp.concatenate([spc, sig], axis=2)
    got = lax.all_to_all(buf, "seq", 0, 0, tiled=True)
    spec_rows = 2 * a_loc * rep
    x = got[:, :, spec_rows:]
    s = got[:, :, :spec_rows].reshape(parts, cpd, 2, a_loc * rep, n2_len).astype(jnp.float32)
    s = s.transpose(2, 1, 0, 3, 4).reshape(2, cpd, n1_len, n2_len)
    gain = lax.dynamic_slice_in_dim(skip_gain, seq_rank * cpd, cpd)
    out = local_conv(x, s, gain, n1_len, km)
    back = out.reshape(cpd, parts, slab).transpose(1, 0, 2)
    back = lax.all_to_all(back, "seq", 0, 0, tiled=True)
    return back.reshape(ch_blk, slab)


def solution(mesh):
    return jax.shard_map(
        per_device,
        mesh=mesh,
        in_specs=(P("chan", "seq"), P(None, "chan", "seq", None), P("chan")),
        out_specs=P("chan", "seq"),
        check_vma=False,
    )
```

```python
import math

import jax
import jax.numpy as jnp
from jax import lax
from jax.sharding import Mesh, PartitionSpec as P

SEQ = ("yh", "z", "core")


def dot_hi(form, left, right):
    return jnp.einsum(form, left, right, precision=lax.Precision.HIGH,
                      preferred_element_type=jnp.float32)


def angle_of(numer, denom):
    return 2.0 * math.pi / denom * (numer % denom).astype(jnp.float32)


def local_conv(x, s, gain, n1_len, km):
    count, length = x.shape
    full_len = 2 * length
    n2_len = full_len // n1_len
    half1 = length // n2_len
    rep = n1_len // km
    rows = jnp.arange(n1_len, dtype=jnp.int32)
    k1 = rows // rep + km * (rows % rep)
    ids2 = jnp.arange(n2_len, dtype=jnp.int32)
    n1 = jnp.arange(half1, dtype=jnp.int32)
    angles = jnp.concatenate([
        angle_of(k1[:, None] * jnp.pad(n1, (0, n2_len - half1))[None, :], n1_len),
        angle_of(ids2[:, None] * ids2[None, :], n2_len),
        angle_of(k1[:, None] * ids2[None, :], full_len),
    ], axis=0)
    tab_c, tab_s = lax.optimization_barrier((jnp.cos(angles), jnp.sin(angles)))
    f1c, f1s = tab_c[:n1_len, :half1], tab_s[:n1_len, :half1]
    wc, ws = tab_c[n1_len:n1_len + n2_len], tab_s[n1_len:n1_len + n2_len]
    tc, ts = tab_c[n1_len + n2_len:], tab_s[n1_len + n2_len:]
    xr = x.reshape(count, half1, n2_len)
    f1 = jnp.stack([f1c, -f1s])
    f1_top = lax.reduce_precision(f1, exponent_bits=8, mantissa_bits=7)
    f1_hi = f1_top.astype(jnp.bfloat16)
    f1_lo = (f1 - f1_top).astype(jnp.bfloat16)
    a = jnp.einsum("hzkn,cnm->hzckm", jnp.stack([f1_hi, f1_lo]), xr,
                   preferred_element_type=jnp.float32)
    ar, ai = a[0, 0] + a[1, 0], a[0, 1] + a[1, 1]
    br = ar * tc + ai * ts
    bi = ai * tc - ar * ts
    w = jnp.stack([wc, ws])
    xf = dot_hi("zckn,wnj->zwckj", jnp.stack([br, bi]), w)
    xfr = xf[0, 0] + xf[1, 1]
    xfi = xf[1, 0] - xf[0, 1]
    pr = xfr * s[0] - xfi * s[1]
    pi = xfr * s[1] + xfi * s[0]
    q = dot_hi("zckj,wjn->zwckn", jnp.stack([pr, pi]), w)
    qr = q[0, 0] - q[1, 1]
    qi = q[1, 0] + q[0, 1]
    rr = qr * tc - qi * ts
    ri = qi * tc + qr * ts
    y = dot_hi("zkn,zckm->cnm", jnp.stack([f1c, -f1s]), jnp.stack([rr, ri]))
    y = y.reshape(count, length) * (1.0 / full_len)
    return (y + gain[:, None] * x.astype(jnp.float32)).astype(jnp.bfloat16)


def per_device(signal, spectrum, skip_gain):
    ch_blk, slab = signal.shape
    parts = lax.axis_size(SEQ)
    cpd = ch_blk // parts
    a_loc, nb = spectrum.shape[2], spectrum.shape[3]
    km = parts * a_loc
    full_len = 2 * parts * slab
    n1_len = 1 << (int(math.log2(full_len)) // 2)
    n2_len = full_len // n1_len
    rep = n1_len // km
    seq_rank = lax.axis_index(SEQ)
    cols = jnp.arange(nb, dtype=jnp.int32)
    perm = cols[:, None] == (cols[None, :] % n2_len) * rep + cols[None, :] // n2_len
    spc = jnp.einsum("rcab,bq->rcaq", spectrum, perm.astype(jnp.bfloat16),
                     preferred_element_type=jnp.float32).astype(jnp.bfloat16)
    spc = spc.reshape(2, parts, cpd, a_loc * rep, n2_len).transpose(1, 2, 0, 3, 4)
    spc = spc.reshape(parts, cpd, 2 * a_loc * rep, n2_len)
    sig = signal.reshape(parts, cpd, slab // n2_len, n2_len)
    buf = jnp.concatenate([spc, sig], axis=2)
    cores = lax.axis_size("core")
    buf = buf.reshape((parts // cores, cores) + buf.shape[1:])
    buf = lax.all_to_all(buf, "core", 1, 1, tiled=True)
    got = lax.all_to_all(buf, ("yh", "z"), 0, 0, tiled=True).reshape((parts,) + buf.shape[2:])
    spec_rows = 2 * a_loc * rep
    x = got[:, :, spec_rows:].transpose(1, 0, 2, 3).reshape(cpd, parts * slab)
    s = got[:, :, :spec_rows].reshape(parts, cpd, 2, a_loc * rep, n2_len).astype(jnp.float32)
    s = s.transpose(2, 1, 0, 3, 4).reshape(2, cpd, n1_len, n2_len)
    gain = lax.dynamic_slice_in_dim(skip_gain, seq_rank * cpd, cpd)
    out = local_conv(x, s, gain, n1_len, km)
    back = out.reshape(cpd, parts, slab).transpose(1, 0, 2)
    back = lax.all_to_all(back, SEQ, 0, 0, tiled=True)
    return back.reshape(ch_blk, slab)


def solution(mesh):
    seq_n, chan_n = mesh.devices.shape
    cores = 2
    fine = Mesh(mesh.devices.reshape(2, seq_n // (2 * cores), cores, chan_n),
                ("yh", "z", "core", "chan"))
    return jax.shard_map(
        per_device,
        mesh=fine,
        in_specs=(P("chan", SEQ), P(None, "chan", SEQ, None), P("chan")),
        out_specs=P("chan", SEQ),
        check_vma=False,
    )
```

```python
import math

import jax
import jax.numpy as jnp
from jax import lax
from jax.sharding import PartitionSpec as P


def dot_hi(form, left, right):
    return jnp.einsum(form, left, right, precision=lax.Precision.HIGH,
                      preferred_element_type=jnp.float32)


def angle_of(numer, denom):
    return 2.0 * math.pi / denom * (numer % denom).astype(jnp.float32)


def local_conv(x, s, gain, n1_len, km):
    count, length = x.shape
    full_len = 2 * length
    n2_len = full_len // n1_len
    half1 = length // n2_len
    rep = n1_len // km
    rows = jnp.arange(n1_len, dtype=jnp.int32)
    k1 = rows // rep + km * (rows % rep)
    ids2 = jnp.arange(n2_len, dtype=jnp.int32)
    n1 = jnp.arange(half1, dtype=jnp.int32)
    angles = jnp.concatenate([
        angle_of(k1[:, None] * jnp.pad(n1, (0, n2_len - half1))[None, :], n1_len),
        angle_of(ids2[:, None] * ids2[None, :], n2_len),
        angle_of(k1[:, None] * ids2[None, :], full_len),
    ], axis=0)
    tab_c, tab_s = lax.optimization_barrier((jnp.cos(angles), jnp.sin(angles)))
    f1c, f1s = tab_c[:n1_len, :half1], tab_s[:n1_len, :half1]
    wc, ws = tab_c[n1_len:n1_len + n2_len], tab_s[n1_len:n1_len + n2_len]
    tc, ts = tab_c[n1_len + n2_len:], tab_s[n1_len + n2_len:]
    xr = x.reshape(count, half1, n2_len)
    f1 = jnp.stack([f1c, -f1s])
    f1_top = lax.reduce_precision(f1, exponent_bits=8, mantissa_bits=7)
    f1_hi = f1_top.astype(jnp.bfloat16)
    f1_lo = (f1 - f1_top).astype(jnp.bfloat16)
    a = jnp.einsum("hzkn,cnm->hzckm", jnp.stack([f1_hi, f1_lo]), xr,
                   preferred_element_type=jnp.float32)
    ar, ai = a[0, 0] + a[1, 0], a[0, 1] + a[1, 1]
    br = ar * tc + ai * ts
    bi = ai * tc - ar * ts
    w = jnp.stack([wc, ws])
    xf = dot_hi("zckn,wnj->zwckj", jnp.stack([br, bi]), w)
    xfr = xf[0, 0] + xf[1, 1]
    xfi = xf[1, 0] - xf[0, 1]
    pr = xfr * s[0] - xfi * s[1]
    pi = xfr * s[1] + xfi * s[0]
    q = dot_hi("zckj,wjn->zwckn", jnp.stack([pr, pi]), w)
    qr = q[0, 0] - q[1, 1]
    qi = q[1, 0] + q[0, 1]
    rr = qr * tc - qi * ts
    ri = qi * tc + qr * ts
    y = dot_hi("zkn,zckm->cnm", jnp.stack([f1c, -f1s]), jnp.stack([rr, ri]))
    y = y.reshape(count, length) * (1.0 / full_len)
    return (y + gain[:, None] * x.astype(jnp.float32)).astype(jnp.bfloat16)


def per_device(signal, spectrum, skip_gain):
    ch_blk, slab = signal.shape
    parts = lax.axis_size("seq")
    cpd = ch_blk // parts
    a_loc, nb = spectrum.shape[2], spectrum.shape[3]
    km = parts * a_loc
    full_len = 2 * parts * slab
    n1_len = 1 << (int(math.log2(full_len)) // 2)
    n2_len = full_len // n1_len
    rep = n1_len // km
    seq_rank = lax.axis_index("seq")
    cols = jnp.arange(nb, dtype=jnp.int32)
    perm = cols[:, None] == (cols[None, :] % n2_len) * rep + cols[None, :] // n2_len
    spc = jnp.einsum("rcab,bq->rcaq", spectrum, perm.astype(jnp.bfloat16),
                     preferred_element_type=jnp.float32).astype(jnp.bfloat16)
    spc = spc.reshape(2, parts, cpd, a_loc * rep, n2_len).transpose(1, 2, 0, 3, 4)
    spc = spc.reshape(parts, cpd, 2 * a_loc * rep, n2_len)
    sig = signal.reshape(parts, cpd, slab // n2_len, n2_len)
    buf = jnp.concatenate([spc, sig], axis=2)
    got = lax.all_to_all(buf, "seq", 0, 0, tiled=True)
    spec_rows = 2 * a_loc * rep
    x = got[:, :, spec_rows:].transpose(1, 0, 2, 3).reshape(cpd, parts * slab)
    half_rows = spec_rows // 2
    s = [got[:, :, h * half_rows:(h + 1) * half_rows].astype(jnp.float32)
         .transpose(1, 0, 2, 3).reshape(cpd, n1_len, n2_len) for h in range(2)]
    gain = lax.dynamic_slice_in_dim(skip_gain, seq_rank * cpd, cpd)
    out = local_conv(x, s, gain, n1_len, km)
    back = out.reshape(cpd, parts, slab).transpose(1, 0, 2)
    back = lax.all_to_all(back, "seq", 0, 0, tiled=True)
    return back.reshape(ch_blk, slab)


def solution(mesh):
    return jax.shard_map(
        per_device,
        mesh=mesh,
        in_specs=(P("chan", "seq"), P(None, "chan", "seq", None), P("chan")),
        out_specs=P("chan", "seq"),
        check_vma=False,
    )
```

```python
import math

import jax
import jax.numpy as jnp
from jax import lax
from jax.sharding import PartitionSpec as P


def dot_hi(form, left, right):
    return jnp.einsum(form, left, right, precision=lax.Precision.HIGH,
                      preferred_element_type=jnp.float32)


def angle_of(numer, denom):
    return 2.0 * math.pi / denom * (numer % denom).astype(jnp.float32)


def local_conv(x, s, gain, n1_len, km):
    n2_len = s[0].shape[2]
    parts, count = x.shape[0], x.shape[1]
    length = parts * x.shape[2] * x.shape[3]
    full_len = 2 * length
    half1 = length // n2_len
    rep = n1_len // km
    rows = jnp.arange(n1_len, dtype=jnp.int32)
    k1 = rows // rep + km * (rows % rep)
    ids2 = jnp.arange(n2_len, dtype=jnp.int32)
    n1 = jnp.arange(half1, dtype=jnp.int32)
    angles = jnp.concatenate([
        angle_of(k1[:, None] * jnp.pad(n1, (0, n2_len - half1))[None, :], n1_len),
        angle_of(ids2[:, None] * ids2[None, :], n2_len),
        angle_of(k1[:, None] * ids2[None, :], full_len),
    ], axis=0)
    tab_c, tab_s = lax.optimization_barrier((jnp.cos(angles), jnp.sin(angles)))
    f1c, f1s = tab_c[:n1_len, :half1], tab_s[:n1_len, :half1]
    wc, ws = tab_c[n1_len:n1_len + n2_len], tab_s[n1_len:n1_len + n2_len]
    tc, ts = tab_c[n1_len + n2_len:], tab_s[n1_len + n2_len:]
    xr = x
    f1 = jnp.stack([f1c, -f1s])
    f1_top = lax.reduce_precision(f1, exponent_bits=8, mantissa_bits=7)
    f1_hi = f1_top.astype(jnp.bfloat16)
    f1_lo = (f1 - f1_top).astype(jnp.bfloat16)
    f1_hl = jnp.stack([f1_hi, f1_lo]).reshape(2, 2, n1_len, parts, half1 // parts)
    a = jnp.einsum("hzkpi,pcim->hzckm", f1_hl, xr, preferred_element_type=jnp.float32)
    ar, ai = a[0, 0] + a[1, 0], a[0, 1] + a[1, 1]
    br = ar * tc + ai * ts
    bi = ai * tc - ar * ts
    w = jnp.stack([wc, ws])
    xf = dot_hi("zckn,wnj->zwckj", jnp.stack([br, bi]), w)
    xfr = xf[0, 0] + xf[1, 1]
    xfi = xf[1, 0] - xf[0, 1]
    pr = xfr * s[0] - xfi * s[1]
    pi = xfr * s[1] + xfi * s[0]
    q = dot_hi("zckj,wjn->zwckn", jnp.stack([pr, pi]), w)
    qr = q[0, 0] - q[1, 1]
    qi = q[1, 0] + q[0, 1]
    rr = qr * tc - qi * ts
    ri = qi * tc + qr * ts
    y = dot_hi("zkn,zckm->cnm", jnp.stack([f1c, -f1s]), jnp.stack([rr, ri]))
    y = y.reshape(count, length) * (1.0 / full_len)
    xs = x.transpose(1, 0, 2, 3).reshape(count, length).astype(jnp.float32)
    return (y + gain[:, None] * xs).astype(jnp.bfloat16)


def per_device(signal, spectrum, skip_gain):
    ch_blk, slab = signal.shape
    parts = lax.axis_size("seq")
    cpd = ch_blk // parts
    a_loc, nb = spectrum.shape[2], spectrum.shape[3]
    km = parts * a_loc
    full_len = 2 * parts * slab
    n1_len = 1 << (int(math.log2(full_len)) // 2)
    n2_len = full_len // n1_len
    rep = n1_len // km
    seq_rank = lax.axis_index("seq")
    cols = jnp.arange(nb, dtype=jnp.int32)
    perm = cols[:, None] == (cols[None, :] % n2_len) * rep + cols[None, :] // n2_len
    spc = jnp.einsum("rcab,bq->rcaq", spectrum, perm.astype(jnp.bfloat16),
                     preferred_element_type=jnp.float32).astype(jnp.bfloat16)
    spc = spc.reshape(2, parts, cpd, a_loc * rep, n2_len).transpose(1, 2, 0, 3, 4)
    spc = spc.reshape(parts, cpd, 2 * a_loc * rep, n2_len)
    sig = signal.reshape(parts, cpd, slab // n2_len, n2_len)
    buf = jnp.concatenate([spc, sig], axis=2)
    got = lax.all_to_all(buf, "seq", 0, 0, tiled=True)
    spec_rows = 2 * a_loc * rep
    x = got[:, :, spec_rows:]
    half_rows = spec_rows // 2
    s = [got[:, :, h * half_rows:(h + 1) * half_rows].astype(jnp.float32)
         .transpose(1, 0, 2, 3).reshape(cpd, n1_len, n2_len) for h in range(2)]
    gain = lax.dynamic_slice_in_dim(skip_gain, seq_rank * cpd, cpd)
    out = local_conv(x, s, gain, n1_len, km)
    back = out.reshape(cpd, parts, slab).transpose(1, 0, 2)
    back = lax.all_to_all(back, "seq", 0, 0, tiled=True)
    return back.reshape(ch_blk, slab)


def solution(mesh):
    return jax.shard_map(
        per_device,
        mesh=mesh,
        in_specs=(P("chan", "seq"), P(None, "chan", "seq", None), P("chan")),
        out_specs=P("chan", "seq"),
        check_vma=False,
    )
```

```python
import math

import jax
import jax.numpy as jnp
from jax import lax
from jax.sharding import PartitionSpec as P


def dot_hi(form, left, right):
    return jnp.einsum(form, left, right, precision=lax.Precision.HIGH,
                      preferred_element_type=jnp.float32)


def angle_of(numer, denom):
    return 2.0 * math.pi / denom * (numer % denom).astype(jnp.float32)


def local_conv(x, s, gain, n1_len, km):
    count, length = x.shape
    full_len = 2 * length
    n2_len = full_len // n1_len
    half1 = length // n2_len
    rep = n1_len // km
    rows = jnp.arange(n1_len, dtype=jnp.int32)
    k1 = rows // rep + km * (rows % rep)
    ids2 = jnp.arange(n2_len, dtype=jnp.int32)
    n1 = jnp.arange(half1, dtype=jnp.int32)
    angles = jnp.concatenate([
        angle_of(k1[:, None] * jnp.pad(n1, (0, n2_len - half1))[None, :], n1_len),
        angle_of(ids2[:, None] * ids2[None, :], n2_len),
        angle_of(k1[:, None] * ids2[None, :], full_len),
    ], axis=0)
    tab_c, tab_s = lax.optimization_barrier((jnp.cos(angles), jnp.sin(angles)))
    f1c, f1s = tab_c[:n1_len, :half1], tab_s[:n1_len, :half1]
    wc, ws = tab_c[n1_len:n1_len + n2_len], tab_s[n1_len:n1_len + n2_len]
    tc, ts = tab_c[n1_len + n2_len:], tab_s[n1_len + n2_len:]
    xr = x.reshape(count, half1, n2_len)
    f1 = jnp.stack([f1c, -f1s])
    f1_top = lax.reduce_precision(f1, exponent_bits=8, mantissa_bits=7)
    f1_hi = f1_top.astype(jnp.bfloat16)
    f1_lo = (f1 - f1_top).astype(jnp.bfloat16)
    a = jnp.einsum("hzkn,cnm->hzckm", jnp.stack([f1_hi, f1_lo]), xr,
                   preferred_element_type=jnp.float32)
    ar, ai = a[0, 0] + a[1, 0], a[0, 1] + a[1, 1]
    br = ar * tc + ai * ts
    bi = ai * tc - ar * ts
    w = jnp.stack([wc, ws])
    xf = dot_hi("zckn,wnj->zwckj", jnp.stack([br, bi]), w)
    xfr = xf[0, 0] + xf[1, 1]
    xfi = xf[1, 0] - xf[0, 1]
    pr = xfr * s[0] - xfi * s[1]
    pi = xfr * s[1] + xfi * s[0]
    q = dot_hi("zckj,wjn->zwckn", jnp.stack([pr, pi]), w)
    qr = q[0, 0] - q[1, 1]
    qi = q[1, 0] + q[0, 1]
    rr = qr * tc - qi * ts
    ri = qi * tc + qr * ts
    y = dot_hi("zkn,zckm->cnm", jnp.stack([f1c, -f1s]), jnp.stack([rr, ri]))
    y = y.reshape(count, length) * (1.0 / full_len)
    return (y + gain[:, None] * x.astype(jnp.float32)).astype(jnp.bfloat16)


def per_device(signal, spectrum, skip_gain):
    ch_blk, slab = signal.shape
    parts = lax.axis_size("seq")
    cpd = ch_blk // parts
    a_loc, nb = spectrum.shape[2], spectrum.shape[3]
    km = parts * a_loc
    full_len = 2 * parts * slab
    n1_len = 1 << (int(math.log2(full_len)) // 2)
    n2_len = full_len // n1_len
    rep = n1_len // km
    seq_rank = lax.axis_index("seq")
    cols = jnp.arange(nb, dtype=jnp.int32)
    perm = cols[:, None] == (cols[None, :] % n2_len) * rep + cols[None, :] // n2_len
    spc = jnp.einsum("rcab,bq->rcaq", spectrum, perm.astype(jnp.bfloat16),
                     preferred_element_type=jnp.float32).astype(jnp.bfloat16)
    spc = spc.reshape(2, parts, cpd, a_loc * rep, n2_len).transpose(1, 2, 0, 3, 4)
    spc = spc.reshape(parts, cpd, 2 * a_loc * rep, n2_len)
    sig = signal.reshape(parts, cpd, slab // n2_len, n2_len)
    buf = jnp.concatenate([sig, spc], axis=2)
    got = lax.all_to_all(buf, "seq", 0, 0, tiled=True)
    spec_rows = 2 * a_loc * rep
    sig_rows = slab // n2_len
    x = got[:, :, :sig_rows].transpose(1, 0, 2, 3).reshape(cpd, parts * slab)
    half_rows = spec_rows // 2
    s = [got[:, :, sig_rows + h * half_rows:sig_rows + (h + 1) * half_rows].astype(jnp.float32)
         .transpose(1, 0, 2, 3).reshape(cpd, n1_len, n2_len) for h in range(2)]
    gain = lax.dynamic_slice_in_dim(skip_gain, seq_rank * cpd, cpd)
    out = local_conv(x, s, gain, n1_len, km)
    back = out.reshape(cpd, parts, slab).transpose(1, 0, 2)
    back = lax.all_to_all(back, "seq", 0, 0, tiled=True)
    return back.reshape(ch_blk, slab)


def solution(mesh):
    return jax.shard_map(
        per_device,
        mesh=mesh,
        in_specs=(P("chan", "seq"), P(None, "chan", "seq", None), P("chan")),
        out_specs=P("chan", "seq"),
        check_vma=False,
    )
```

```python
import math

import jax
import jax.numpy as jnp
from jax import lax
from jax.sharding import PartitionSpec as P


def dot_hi(form, left, right):
    return jnp.einsum(form, left, right, precision=lax.Precision.HIGH,
                      preferred_element_type=jnp.float32)


def angle_of(numer, denom):
    return 2.0 * math.pi / denom * (numer % denom).astype(jnp.float32)


def local_conv(x, s, gain, n1_len, km):
    count, length = x.shape
    full_len = 2 * length
    n2_len = full_len // n1_len
    half1 = length // n2_len
    rep = n1_len // km
    rows = jnp.arange(n1_len, dtype=jnp.int32)
    k1 = rows // rep + km * (rows % rep)
    ids2 = jnp.arange(n2_len, dtype=jnp.int32)
    n1 = jnp.arange(half1, dtype=jnp.int32)
    angles = jnp.concatenate([
        angle_of(k1[:, None] * jnp.pad(n1, (0, n2_len - half1))[None, :], n1_len),
        angle_of(ids2[:, None] * ids2[None, :], n2_len),
        angle_of(k1[:, None] * ids2[None, :], full_len),
    ], axis=0)
    tab_c, tab_s = lax.optimization_barrier((jnp.cos(angles), jnp.sin(angles)))
    f1c, f1s = tab_c[:n1_len, :half1], tab_s[:n1_len, :half1]
    wc, ws = tab_c[n1_len:n1_len + n2_len], tab_s[n1_len:n1_len + n2_len]
    tc, ts = tab_c[n1_len + n2_len:], tab_s[n1_len + n2_len:]
    xr = x.reshape(count, half1, n2_len)
    f1 = jnp.stack([f1c, -f1s])
    f1_top = lax.reduce_precision(f1, exponent_bits=8, mantissa_bits=7)
    f1_hi = f1_top.astype(jnp.bfloat16)
    f1_lo = (f1 - f1_top).astype(jnp.bfloat16)
    a = jnp.einsum("hzkn,cnm->hzckm", jnp.stack([f1_hi, f1_lo]), xr,
                   preferred_element_type=jnp.float32)
    ar, ai = a[0, 0] + a[1, 0], a[0, 1] + a[1, 1]
    br = ar * tc + ai * ts
    bi = ai * tc - ar * ts
    w = jnp.stack([wc, ws])
    xf = dot_hi("zckn,wnj->zwckj", jnp.stack([br, bi]), w)
    xfr = xf[0, 0] + xf[1, 1]
    xfi = xf[1, 0] - xf[0, 1]
    pr = xfr * s[0] - xfi * s[1]
    pi = xfr * s[1] + xfi * s[0]
    q = dot_hi("zckj,wjn->zwckn", jnp.stack([pr, pi]), w)
    qr = q[0, 0] - q[1, 1]
    qi = q[1, 0] + q[0, 1]
    rr = qr * tc - qi * ts
    ri = qi * tc + qr * ts
    y = dot_hi("zkn,zckm->cnm", jnp.stack([f1c, -f1s]), jnp.stack([rr, ri]))
    y = y.reshape(count, length) * (1.0 / full_len)
    return (y + gain[:, None] * x.astype(jnp.float32)).astype(jnp.bfloat16)


def per_device(signal, spectrum, skip_gain):
    ch_blk, slab = signal.shape
    parts = lax.axis_size("seq")
    cpd = ch_blk // parts
    a_loc, nb = spectrum.shape[2], spectrum.shape[3]
    km = parts * a_loc
    full_len = 2 * parts * slab
    n1_len = 1 << (int(math.log2(full_len)) // 2)
    n2_len = full_len // n1_len
    rep = n1_len // km
    seq_rank = lax.axis_index("seq")
    cols = jnp.arange(nb, dtype=jnp.int32)
    perm = cols[:, None] == (cols[None, :] % n2_len) * rep + cols[None, :] // n2_len
    spc = jnp.dot(spectrum.reshape(-1, nb), perm.astype(jnp.bfloat16),
                  preferred_element_type=jnp.bfloat16)
    spc = spc.reshape(2, parts, cpd, a_loc * rep, n2_len).transpose(1, 2, 0, 3, 4)
    spc = spc.reshape(parts, cpd, 2 * a_loc * rep, n2_len)
    sig = signal.reshape(parts, cpd, slab // n2_len, n2_len)
    buf = jnp.concatenate([spc, sig], axis=2)
    got = lax.all_to_all(buf, "seq", 0, 0, tiled=True)
    spec_rows = 2 * a_loc * rep
    x = got[:, :, spec_rows:].transpose(1, 0, 2, 3).reshape(cpd, parts * slab)
    half_rows = spec_rows // 2
    s = [got[:, :, h * half_rows:(h + 1) * half_rows].astype(jnp.float32)
         .transpose(1, 0, 2, 3).reshape(cpd, n1_len, n2_len) for h in range(2)]
    gain = lax.dynamic_slice_in_dim(skip_gain, seq_rank * cpd, cpd)
    out = local_conv(x, s, gain, n1_len, km)
    back = out.reshape(cpd, parts, slab).transpose(1, 0, 2)
    back = lax.all_to_all(back, "seq", 0, 0, tiled=True)
    return back.reshape(ch_blk, slab)


def solution(mesh):
    return jax.shard_map(
        per_device,
        mesh=mesh,
        in_specs=(P("chan", "seq"), P(None, "chan", "seq", None), P("chan")),
        out_specs=P("chan", "seq"),
        check_vma=False,
    )
```

```python
import math

import jax
import jax.numpy as jnp
from jax import lax
from jax.sharding import PartitionSpec as P


def dot_hi(form, left, right):
    return jnp.einsum(form, left, right, precision=lax.Precision.HIGH,
                      preferred_element_type=jnp.float32)


def angle_of(numer, denom):
    return 2.0 * math.pi / denom * (numer % denom).astype(jnp.float32)


def local_conv(x, s, gain, n1_len, km):
    count, length = x.shape
    full_len = 2 * length
    n2_len = full_len // n1_len
    half1 = length // n2_len
    rep = n1_len // km
    rows = jnp.arange(n1_len, dtype=jnp.int32)
    k1 = rows // rep + km * (rows % rep)
    ids2 = jnp.arange(n2_len, dtype=jnp.int32)
    n1 = jnp.arange(half1, dtype=jnp.int32)
    angles = jnp.concatenate([
        angle_of(k1[:, None] * jnp.pad(n1, (0, n2_len - half1))[None, :], n1_len),
        angle_of(ids2[:, None] * ids2[None, :], n2_len),
        angle_of(k1[:, None] * ids2[None, :], full_len),
    ], axis=0)
    tab_c, tab_s = lax.optimization_barrier((jnp.cos(angles), jnp.sin(angles)))
    f1c, f1s = tab_c[:n1_len, :half1], tab_s[:n1_len, :half1]
    wc, ws = tab_c[n1_len:n1_len + n2_len], tab_s[n1_len:n1_len + n2_len]
    tc, ts = tab_c[n1_len + n2_len:], tab_s[n1_len + n2_len:]
    xr = x.reshape(count, half1, n2_len)
    f1 = jnp.stack([f1c, -f1s])
    f1_top = lax.reduce_precision(f1, exponent_bits=8, mantissa_bits=7)
    f1_hi = f1_top.astype(jnp.bfloat16)
    f1_lo = (f1 - f1_top).astype(jnp.bfloat16)
    a = jnp.einsum("hzkn,cnm->hzckm", jnp.stack([f1_hi, f1_lo]), xr,
                   preferred_element_type=jnp.float32)
    ar, ai = a[0, 0] + a[1, 0], a[0, 1] + a[1, 1]
    br = ar * tc + ai * ts
    bi = ai * tc - ar * ts
    w = jnp.stack([wc, ws])
    xf = dot_hi("zckn,wnj->zwckj", jnp.stack([br, bi]), w)
    xfr = xf[0, 0] + xf[1, 1]
    xfi = xf[1, 0] - xf[0, 1]
    pr = xfr * s[0] - xfi * s[1]
    pi = xfr * s[1] + xfi * s[0]
    q = dot_hi("zckj,wjn->zwckn", jnp.stack([pr, pi]), w)
    qr = q[0, 0] - q[1, 1]
    qi = q[1, 0] + q[0, 1]
    rr = qr * tc - qi * ts
    ri = qi * tc + qr * ts
    y = dot_hi("zkn,zckm->cnm", jnp.stack([f1c, -f1s]), jnp.stack([rr, ri]))
    y = y.reshape(count, length) * (1.0 / full_len)
    return (y + gain[:, None] * x.astype(jnp.float32)).astype(jnp.bfloat16)


def per_device(signal, spectrum, skip_gain):
    ch_blk, slab = signal.shape
    parts = lax.axis_size("seq")
    cpd = ch_blk // parts
    a_loc, nb = spectrum.shape[2], spectrum.shape[3]
    km = parts * a_loc
    full_len = 2 * parts * slab
    n1_len = 1 << (int(math.log2(full_len)) // 2)
    n2_len = full_len // n1_len
    rep = n1_len // km
    seq_rank = lax.axis_index("seq")
    cols = jnp.arange(nb, dtype=jnp.int32)
    perm = cols[:, None] == (cols[None, :] % n2_len) * rep + cols[None, :] // n2_len
    spc = jnp.dot(spectrum.reshape(-1, nb), perm.astype(jnp.bfloat16),
                  preferred_element_type=jnp.bfloat16)
    spc = spc.reshape(2, parts, cpd, a_loc * rep, n2_len).transpose(1, 2, 0, 3, 4)
    spc = spc.reshape(parts, cpd, 2 * a_loc * rep, n2_len)
    sig = signal.reshape(parts, cpd, slab // n2_len, n2_len)
    buf = jnp.concatenate([spc, sig], axis=2)
    rows_per = buf.shape[2]
    buf = buf.reshape(parts, cpd * rows_per, n2_len)
    got = lax.all_to_all(buf, "seq", 0, 0, tiled=True).reshape(parts, cpd, rows_per, n2_len)
    spec_rows = 2 * a_loc * rep
    x = got[:, :, spec_rows:].transpose(1, 0, 2, 3).reshape(cpd, parts * slab)
    half_rows = spec_rows // 2
    s = [got[:, :, h * half_rows:(h + 1) * half_rows].astype(jnp.float32)
         .transpose(1, 0, 2, 3).reshape(cpd, n1_len, n2_len) for h in range(2)]
    gain = lax.dynamic_slice_in_dim(skip_gain, seq_rank * cpd, cpd)
    out = local_conv(x, s, gain, n1_len, km)
    back = out.reshape(cpd, parts, slab).transpose(1, 0, 2)
    back = lax.all_to_all(back, "seq", 0, 0, tiled=True)
    return back.reshape(ch_blk, slab)


def solution(mesh):
    return jax.shard_map(
        per_device,
        mesh=mesh,
        in_specs=(P("chan", "seq"), P(None, "chan", "seq", None), P("chan")),
        out_specs=P("chan", "seq"),
        check_vma=False,
    )
```
